512 devices in a mesh: tm: 32 (over y, z_lo), space: 16 (over x, z_hi, core).
Axes of the slice: x: 4, y: 8, z: 8 (z_hi: 2, z_lo: 4; z = z_hi * 4 + z_lo), core: 2. Of those that a mesh axis runs over, the one named last changes fastest.
Arguments:
- prior_adjoint_iterate: float32 [32, 256, 128, 128], P('tm', 'space'), may hold values from -6 to 6
- material: int32 [256, 128, 128], P('space'), may hold values from 0 to 7
- probe_cell_index: int32 [1024], P('space'), may hold values from 0 to 4194303, as said below
- misfit: float32 [32, 1024], P('tm', 'space'), may hold values from -12 to 12
- ventilation_heat_loss: float32 [32], P('tm'), as said below
- conductance: float32 [8], replicated, may hold values from 0.03 to 0.14
- rock_heat_drain: float32 [8], replicated, as said below
Outputs:
- adjoint_new: float32 [32, 256, 128, 128], P('tm', 'space')
The draws below stay inside these ranges and needn't reach their ends.
Inputs may be any that keep to these rules, and one draw needn't show every extreme that they name: `probe_cell_index`: sensors 64 p to 64 (p + 1) - 1 lie in the p-th block of 16 planes of the first dimension; a cell may hold several sensors. `ventilation_heat_loss`: Non-negative. `rock_heat_drain`: Positive.
All inputs are finite; a program needn't handle non-finite values.
Results may differ from the reference program's by a relative error of at most 0.00002.
Values sent between devices are 32-bit elements; how exact they have to be, the bound alone decides.
No kernel may reach another device: no remote copies, remote signals or barrier semaphores. Data moves between devices by JAX's collectives and lax.ppermute only.
A program may use at most 64 MiB of HBM per device.

```python
import math
import jax
import jax.numpy as jnp

CX = 16
NY = 128
NZ = 128
FINE_STEPS = 4
MATS = 8
SENS_DEV = 64
SLABS = 32
NX = 256
SENS = 1024


def draw_probe_cell_index(key, part):
    number = jnp.arange(SENS, dtype=jnp.int32)
    tiles = number // SENS_DEV
    offset = jax.random.randint(key, (SENS,), 0, CX * NY * NZ, dtype=jnp.int32)
    offset = jnp.where(number == 0, 0, offset)
    offset = jnp.where(number == SENS - 1, CX * NY * NZ - 1, offset)
    return (tiles * (CX * NY * NZ) + offset).astype(jnp.int32)


def draw_rock_heat_drain(key, part):
    spread = jax.random.uniform(jax.random.fold_in(key, 11), (MATS,), jnp.float32)
    lower, upper = (0.0001, 0.06)
    return jnp.exp(jnp.log(lower) + spread * (jnp.log(upper) - jnp.log(lower))).astype(jnp.float32)


def draw_ventilation_heat_loss(key, part):
    count = max(1, SLABS // 8)
    order = jax.random.permutation(jax.random.fold_in(key, 21), SLABS)
    strength = jax.random.uniform(jax.random.fold_in(key, 22), (SLABS,), jnp.float32, 0.05, 0.15)
    return jnp.where(order < count, strength, 0.0).astype(jnp.float32)


def plant(result, rng, least, high):
    longest = result.shape.index(max(result.shape))
    spots = []
    for shift in (0, 1):
        where = [jax.random.randint(jax.random.fold_in(rng, axis), (), 0, length) for axis, length in enumerate(result.shape)]
        where[longest] = (where[longest] + shift) % result.shape[longest]
        spots.append(tuple(where))
    return result.at[spots[0]].set(least).at[spots[1]].set(high)


def block_levels(key, dims, pieces, least, largest):
    def one(dim, shards_of):
        heights = jax.random.uniform(jax.random.fold_in(jax.random.fold_in(key, 6), dim), (shards_of,), jnp.float32, least / len(pieces), largest / len(pieces))
        return jnp.repeat(jnp.exp(heights), dims[dim] // shards_of).reshape((-1,) + (1,) * (len(dims) - dim - 1))

    factor_of = one(*pieces[0])
    for cut in pieces[1:]:
        factor_of = factor_of * one(*cut)
    return factor_of


def noise(own_key, dims, deviation, bound, cuts=(), held_as=jnp.bfloat16):
    values = jax.random.normal(own_key, dims, jnp.float32) * deviation
    if len(cuts) > 0:
        values = block_levels(own_key, dims, cuts, -0.22, 0.18) * values
    return jnp.clip(values, min=-bound, max=bound).astype(held_as)


def setup_inputs(seed: int = 0) -> dict:
    streams_of = jax.random.split(jax.random.key(seed), 8)
    prior_adjoint_iterate = noise(streams_of[0], (SLABS, NX, NY, NZ), 1.0, 6.0, ((0, 32), (1, 16)), jnp.float32)
    material = plant(jax.random.randint(streams_of[1], (NX, NY, NZ), 0, MATS), jax.random.fold_in(streams_of[1], 1), 0, MATS - 1).astype(jnp.int32)
    probe_cell_index = draw_probe_cell_index(jax.random.fold_in(streams_of[7], 71), 0)
    misfit = noise(streams_of[3], (SLABS, SENS), 2.0, 12.0, ((0, 32), (1, 16)), jnp.float32)
    ventilation_heat_loss = draw_ventilation_heat_loss(jax.random.fold_in(streams_of[7], 71), 0)
    conductance = jnp.clip(jnp.exp(jax.random.uniform(streams_of[5], (MATS,), jnp.float32, math.log(0.03), math.log(0.14))), 0.03, 0.14)
    rock_heat_drain = draw_rock_heat_drain(jax.random.fold_in(streams_of[7], 71), 0)
    return {"prior_adjoint_iterate": prior_adjoint_iterate, "material": material, "probe_cell_index": probe_cell_index, "misfit": misfit, "ventilation_heat_loss": ventilation_heat_loss, "conductance": conductance, "rock_heat_drain": rock_heat_drain}


def coarsen(field):
    split = field.reshape(field.shape[0] // 2, 2, field.shape[1] // 2, 2, field.shape[2])
    return 0.25 * ((split[:, 0, :, 0] + split[:, 1, :, 0]) + (split[:, 0, :, 1] + split[:, 1, :, 1]))


def refine(coarse):
    return jnp.repeat(jnp.repeat(coarse, 2, axis=0), 2, axis=1)


def neighbours(padded):
    x_sides = padded[2:, 1:-1, 1:-1] + padded[:-2, 1:-1, 1:-1]
    y_sides = padded[1:-1, 2:, 1:-1] + padded[1:-1, :-2, 1:-1]
    z_sides = padded[1:-1, 1:-1, 2:] + padded[1:-1, 1:-1, :-2]
    return (x_sides + y_sides) + z_sides


def reference(prior_adjoint_iterate, material, probe_cell_index, misfit, ventilation_heat_loss, conductance, rock_heat_drain):
    cond_cell = conductance[material]
    cell_heat_drain = rock_heat_drain[material]
    coarse_heat_drain = coarsen(cell_heat_drain)
    rates = []
    corrections = []
    for window_index in range(SLABS):
        source = jnp.zeros((NX * NY * NZ,), jnp.float32).at[probe_cell_index].add(misfit[window_index]).reshape(NX, NY, NZ)
        drain_amounts = cell_heat_drain + ventilation_heat_loss[window_index]
        current = prior_adjoint_iterate[window_index] + source
        for sweep_index in range(FINE_STEPS):
            weighted = cond_cell * current
            current = current + (neighbours(jnp.pad(weighted, 1)) - 6.0 * weighted) - drain_amounts * current
        coarse_decay_rate = jnp.exp(-FINE_STEPS * (coarse_heat_drain + ventilation_heat_loss[window_index]))
        correction = current - refine(coarse_decay_rate * coarsen(prior_adjoint_iterate[window_index]))
        rates.append(coarse_decay_rate)
        corrections.append(correction)
    chained = coarsen(prior_adjoint_iterate[SLABS - 1])
    outputs = [None] * SLABS
    for window_index in reversed(range(SLABS)):
        outputs[window_index] = refine(rates[window_index] * chained) + corrections[window_index]
        chained = rates[window_index] * chained + coarsen(corrections[window_index])
    return jnp.stack(outputs)
```

```python
import jax
import jax.numpy as jnp
from jax import lax
from jax.sharding import PartitionSpec as P

FINE_STEPS = 4


def padded_2(value, sides, width):
    for axis, dim in sides:
        size, length = (lax.axis_size(axis), value.shape[dim])
        up = [(i, (i + 1) % size) for i in range(size - 1)]
        down = [(j, i) for i, j in up]
        last = lax.slice_in_dim(value, length - width, length, axis=dim)
        initial = lax.slice_in_dim(value, 0, width, axis=dim)
        before = lax.ppermute(last, axis, up)
        after = lax.ppermute(initial, axis, down)
        value = jnp.concatenate([before, value, after], axis=dim)
    return value


def shifted(value, axis, steps):
    count = lax.axis_size(axis)
    initial, last = (max(0, -steps), min(count, count - steps))
    return lax.ppermute(value, axis, [(source, source + steps) for source in range(initial, last)])


def coarsen(field):
    split = field.reshape(field.shape[0] // 2, 2, field.shape[1] // 2, 2, field.shape[2])
    return 0.25 * (split[:, 0, :, 0] + split[:, 1, :, 0] + (split[:, 0, :, 1] + split[:, 1, :, 1]))


def refine(coarse):
    return jnp.repeat(jnp.repeat(coarse, 2, axis=0), 2, axis=1)


def neighbours(padded):
    x_sides = padded[2:, 1:-1, 1:-1] + padded[:-2, 1:-1, 1:-1]
    y_sides = padded[1:-1, 2:, 1:-1] + padded[1:-1, :-2, 1:-1]
    z_sides = padded[1:-1, 1:-1, 2:] + padded[1:-1, 1:-1, :-2]
    return x_sides + y_sides + z_sides


def lookup(material, values):
    summed = jnp.zeros(material.shape, jnp.float32)
    for rock_type in range(values.shape[0]):
        summed = summed + jnp.where(material == rock_type, values[rock_type], 0.0)
    return summed


def on_device(
    prior_adjoint_iterate,
    material,
    probe_cell_index,
    misfit,
    ventilation_heat_loss,
    conductance,
    rock_heat_drain,
):
    adjoint = prior_adjoint_iterate[0]
    planes = adjoint.shape[0]
    across = adjoint.shape[1]
    depth = adjoint.shape[2]
    cond_cell = lookup(material, conductance)
    cell_heat_drain = lookup(material, rock_heat_drain)
    drain_amounts = cell_heat_drain + ventilation_heat_loss[0]
    local_cell = probe_cell_index - lax.axis_index("space") * (planes * across * depth)
    source = (
        jnp.zeros((planes * across * depth,), jnp.float32)
        .at[local_cell]
        .add(misfit[0])
        .reshape(planes, across, depth)
    )
    seeded = adjoint + source
    current = seeded
    for sweep_index in range(FINE_STEPS):
        weighted = cond_cell * current
        padded_x = padded_2(weighted, (("space", 0),), 1)
        padded = jnp.pad(padded_x, ((0, 0), (1, 1), (1, 1)))
        current = current + (neighbours(padded) - 6.0 * weighted) - drain_amounts * current
    coarse_baseline = coarsen(cell_heat_drain)
    coarse_decay_rate = jnp.exp(-FINE_STEPS * (coarse_baseline + ventilation_heat_loss[0]))
    coarse_old = coarsen(adjoint)
    correction = current - refine(coarse_decay_rate * coarse_old)
    reduced = coarsen(correction)
    tm_size = lax.axis_size("tm")
    is_last = lax.axis_index("tm") == tm_size - 1
    per_cell = jnp.exp(-FINE_STEPS * coarse_baseline)
    gain = jnp.exp(-FINE_STEPS * ventilation_heat_loss[0])
    top = coarse_decay_rate * coarse_old + reduced
    total = jnp.where(is_last, top, reduced)
    shape = total.shape
    rows = total.size // shape[-1]
    power = per_cell
    distance = 1
    while distance < tm_size:
        packed = jnp.concatenate(
            [total.reshape(rows, shape[-1]), jnp.broadcast_to(gain, (8, shape[-1]))], axis=0
        )
        arrived = shifted(packed, "tm", -distance)
        total = total + (power * gain) * arrived[:rows].reshape(shape)
        gain = gain * arrived[rows, 0]
        power = power * power
        distance *= 2
    decayed = jnp.where(is_last, coarse_decay_rate * coarse_old, total - reduced)
    adjoint_new = refine(decayed) + correction
    return adjoint_new[None]


def solution(mesh):
    in_specs = (
        P("tm", "space", None, None),
        P("space", None, None),
        P("space"),
        P("tm", "space"),
        P("tm"),
        P(),
        P(),
    )
    out_specs = P("tm", "space", None, None)
    return jax.shard_map(
        on_device, mesh=mesh, in_specs=in_specs, out_specs=out_specs, check_vma=False
    )
```

```python
import jax
import jax.numpy as jnp
from jax import lax
from jax.sharding import PartitionSpec as P

FINE_STEPS = 4


def padded_2(value, sides, width):
    for axis, dim in sides:
        size, length = (lax.axis_size(axis), value.shape[dim])
        up = [(i, (i + 1) % size) for i in range(size - 1)]
        down = [(j, i) for i, j in up]
        last = lax.slice_in_dim(value, length - width, length, axis=dim)
        initial = lax.slice_in_dim(value, 0, width, axis=dim)
        before = lax.ppermute(last, axis, up)
        after = lax.ppermute(initial, axis, down)
        value = jnp.concatenate([before, value, after], axis=dim)
    return value


def shifted(value, axis, steps):
    count = lax.axis_size(axis)
    initial, last = (max(0, -steps), min(count, count - steps))
    return lax.ppermute(value, axis, [(source, source + steps) for source in range(initial, last)])


def coarsen(field):
    split = field.reshape(field.shape[0] // 2, 2, field.shape[1] // 2, 2, field.shape[2])
    return 0.25 * (split[:, 0, :, 0] + split[:, 1, :, 0] + (split[:, 0, :, 1] + split[:, 1, :, 1]))


def refine(coarse):
    return jnp.repeat(jnp.repeat(coarse, 2, axis=0), 2, axis=1)


def neighbours(padded):
    x_sides = padded[2:, 1:-1, 1:-1] + padded[:-2, 1:-1, 1:-1]
    y_sides = padded[1:-1, 2:, 1:-1] + padded[1:-1, :-2, 1:-1]
    z_sides = padded[1:-1, 1:-1, 2:] + padded[1:-1, 1:-1, :-2]
    return x_sides + y_sides + z_sides


def lookup(material, values):
    bits = [(material & (1 << b)) != 0 for b in range(3)]
    level = [values[k] for k in range(values.shape[0])]
    for bit in bits:
        level = [jnp.where(bit, level[k + 1], level[k]) for k in range(0, len(level), 2)]
    return level[0]


def on_device(
    prior_adjoint_iterate,
    material,
    probe_cell_index,
    misfit,
    ventilation_heat_loss,
    conductance,
    rock_heat_drain,
):
    adjoint = prior_adjoint_iterate[0]
    planes = adjoint.shape[0]
    across = adjoint.shape[1]
    depth = adjoint.shape[2]
    cond_cell, cell_heat_drain = lax.optimization_barrier(
        (lookup(material, conductance), lookup(material, rock_heat_drain))
    )
    drain_amounts = cell_heat_drain + ventilation_heat_loss[0]
    local_cell = probe_cell_index - lax.axis_index("space") * (planes * across * depth)
    source = (
        jnp.zeros((planes * across * depth,), jnp.float32)
        .at[local_cell]
        .add(misfit[0])
        .reshape(planes, across, depth)
    )
    seeded = adjoint + source
    current = seeded
    for sweep_index in range(FINE_STEPS):
        weighted = cond_cell * current
        padded_x = padded_2(weighted, (("space", 0),), 1)
        padded = jnp.pad(padded_x, ((0, 0), (1, 1), (1, 1)))
        current = current + (neighbours(padded) - 6.0 * weighted) - drain_amounts * current
    coarse_baseline = coarsen(cell_heat_drain)
    coarse_decay_rate = jnp.exp(-FINE_STEPS * (coarse_baseline + ventilation_heat_loss[0]))
    coarse_old = coarsen(adjoint)
    correction = current - refine(coarse_decay_rate * coarse_old)
    reduced = coarsen(correction)
    tm_size = lax.axis_size("tm")
    is_last = lax.axis_index("tm") == tm_size - 1
    per_cell = jnp.exp(-FINE_STEPS * coarse_baseline)
    gain = jnp.exp(-FINE_STEPS * ventilation_heat_loss[0])
    top = coarse_decay_rate * coarse_old + reduced
    total = jnp.where(is_last, top, reduced)
    shape = total.shape
    rows = total.size // shape[-1]
    power = per_cell
    distance = 1
    while distance < tm_size:
        packed = jnp.concatenate(
            [total.reshape(rows, shape[-1]), jnp.broadcast_to(gain, (8, shape[-1]))], axis=0
        )
        arrived = shifted(packed, "tm", -distance)
        total = total + (power * gain) * arrived[:rows].reshape(shape)
        gain = gain * arrived[rows, 0]
        power = power * power
        distance *= 2
    decayed = jnp.where(is_last, coarse_decay_rate * coarse_old, total - reduced)
    adjoint_new = refine(decayed) + correction
    return adjoint_new[None]


def solution(mesh):
    in_specs = (
        P("tm", "space", None, None),
        P("space", None, None),
        P("space"),
        P("tm", "space"),
        P("tm"),
        P(),
        P(),
    )
    out_specs = P("tm", "space", None, None)
    return jax.shard_map(
        on_device, mesh=mesh, in_specs=in_specs, out_specs=out_specs, check_vma=False
    )
```

```python
import jax
import jax.numpy as jnp
from jax import lax
from jax.experimental import pallas as pl
from jax.experimental.pallas import tpu as pltpu
from jax.sharding import PartitionSpec as P

FINE_STEPS = 4


def padded_2(value, sides, width):
    for axis, dim in sides:
        size, length = (lax.axis_size(axis), value.shape[dim])
        up = [(i, (i + 1) % size) for i in range(size - 1)]
        down = [(j, i) for i, j in up]
        last = lax.slice_in_dim(value, length - width, length, axis=dim)
        initial = lax.slice_in_dim(value, 0, width, axis=dim)
        before = lax.ppermute(last, axis, up)
        after = lax.ppermute(initial, axis, down)
        value = jnp.concatenate([before, value, after], axis=dim)
    return value


def shifted(value, axis, steps):
    count = lax.axis_size(axis)
    initial, last = (max(0, -steps), min(count, count - steps))
    return lax.ppermute(value, axis, [(source, source + steps) for source in range(initial, last)])


def coarsen(field):
    split = field.reshape(field.shape[0] // 2, 2, field.shape[1] // 2, 2, field.shape[2])
    return 0.25 * (split[:, 0, :, 0] + split[:, 1, :, 0] + (split[:, 0, :, 1] + split[:, 1, :, 1]))


def refine(coarse):
    return jnp.repeat(jnp.repeat(coarse, 2, axis=0), 2, axis=1)


def neighbours(padded):
    x_sides = padded[2:, 1:-1, 1:-1] + padded[:-2, 1:-1, 1:-1]
    y_sides = padded[1:-1, 2:, 1:-1] + padded[1:-1, :-2, 1:-1]
    z_sides = padded[1:-1, 1:-1, 2:] + padded[1:-1, 1:-1, :-2]
    return x_sides + y_sides + z_sides


def _select_tree(material, table_ref):
    bits = [(material & (1 << b)) != 0 for b in range(3)]
    level = [table_ref[k] for k in range(8)]
    for bit in bits:
        level = [jnp.where(bit, level[k + 1], level[k]) for k in range(0, len(level), 2)]
    return level[0]


def _lookup_kernel(cond_table, drain_table, material_ref, cond_ref, drain_ref):
    material = material_ref[...]
    cond_ref[...] = _select_tree(material, cond_table)
    drain_ref[...] = _select_tree(material, drain_table)


def lookup_both(material, conductance, rock_heat_drain):
    planes = material.shape[0]
    block = (4,) + material.shape[1:]
    spec = pl.BlockSpec(block, lambda i: (i, 0, 0))
    smem = pl.BlockSpec(memory_space=pltpu.SMEM)
    out = jax.ShapeDtypeStruct(material.shape, jnp.float32)
    return pl.pallas_call(
        _lookup_kernel,
        grid=(planes // block[0],),
        in_specs=[smem, smem, spec],
        out_specs=[spec, spec],
        out_shape=[out, out],
    )(conductance, rock_heat_drain, material)


def on_device(
    prior_adjoint_iterate,
    material,
    probe_cell_index,
    misfit,
    ventilation_heat_loss,
    conductance,
    rock_heat_drain,
):
    adjoint = prior_adjoint_iterate[0]
    planes = adjoint.shape[0]
    across = adjoint.shape[1]
    depth = adjoint.shape[2]
    cond_cell, cell_heat_drain = lookup_both(material, conductance, rock_heat_drain)
    drain_amounts = cell_heat_drain + ventilation_heat_loss[0]
    local_cell = probe_cell_index - lax.axis_index("space") * (planes * across * depth)
    source = (
        jnp.zeros((planes * across * depth,), jnp.float32)
        .at[local_cell]
        .add(misfit[0])
        .reshape(planes, across, depth)
    )
    seeded = adjoint + source
    current = seeded
    for sweep_index in range(FINE_STEPS):
        weighted = cond_cell * current
        padded_x = padded_2(weighted, (("space", 0),), 1)
        padded = jnp.pad(padded_x, ((0, 0), (1, 1), (1, 1)))
        current = current + (neighbours(padded) - 6.0 * weighted) - drain_amounts * current
    coarse_baseline = coarsen(cell_heat_drain)
    coarse_decay_rate = jnp.exp(-FINE_STEPS * (coarse_baseline + ventilation_heat_loss[0]))
    coarse_old = coarsen(adjoint)
    correction = current - refine(coarse_decay_rate * coarse_old)
    reduced = coarsen(correction)
    tm_size = lax.axis_size("tm")
    is_last = lax.axis_index("tm") == tm_size - 1
    per_cell = jnp.exp(-FINE_STEPS * coarse_baseline)
    gain = jnp.exp(-FINE_STEPS * ventilation_heat_loss[0])
    top = coarse_decay_rate * coarse_old + reduced
    total = jnp.where(is_last, top, reduced)
    shape = total.shape
    rows = total.size // shape[-1]
    power = per_cell
    distance = 1
    while distance < tm_size:
        packed = jnp.concatenate(
            [total.reshape(rows, shape[-1]), jnp.broadcast_to(gain, (8, shape[-1]))], axis=0
        )
        arrived = shifted(packed, "tm", -distance)
        total = total + (power * gain) * arrived[:rows].reshape(shape)
        gain = gain * arrived[rows, 0]
        power = power * power
        distance *= 2
    decayed = jnp.where(is_last, coarse_decay_rate * coarse_old, total - reduced)
    adjoint_new = refine(decayed) + correction
    return adjoint_new[None]


def solution(mesh):
    in_specs = (
        P("tm", "space", None, None),
        P("space", None, None),
        P("space"),
        P("tm", "space"),
        P("tm"),
        P(),
        P(),
    )
    out_specs = P("tm", "space", None, None)
    return jax.shard_map(
        on_device, mesh=mesh, in_specs=in_specs, out_specs=out_specs, check_vma=False
    )
```

```python
import jax
import jax.numpy as jnp
from jax import lax
from jax.experimental import pallas as pl
from jax.experimental.pallas import tpu as pltpu
from jax.sharding import PartitionSpec as P

FINE_STEPS = 4


def padded_2(value, sides, width):
    for axis, dim in sides:
        size, length = (lax.axis_size(axis), value.shape[dim])
        up = [(i, (i + 1) % size) for i in range(size - 1)]
        down = [(j, i) for i, j in up]
        last = lax.slice_in_dim(value, length - width, length, axis=dim)
        initial = lax.slice_in_dim(value, 0, width, axis=dim)
        before = lax.ppermute(last, axis, up)
        after = lax.ppermute(initial, axis, down)
        value = jnp.concatenate([before, value, after], axis=dim)
    return value


def shifted(value, axis, steps):
    count = lax.axis_size(axis)
    initial, last = (max(0, -steps), min(count, count - steps))
    return lax.ppermute(value, axis, [(source, source + steps) for source in range(initial, last)])


def coarsen(field):
    split = field.reshape(field.shape[0] // 2, 2, field.shape[1] // 2, 2, field.shape[2])
    return 0.25 * (split[:, 0, :, 0] + split[:, 1, :, 0] + (split[:, 0, :, 1] + split[:, 1, :, 1]))


def refine(coarse):
    return jnp.repeat(jnp.repeat(coarse, 2, axis=0), 2, axis=1)


def neighbours(padded):
    x_sides = padded[2:, 1:-1, 1:-1] + padded[:-2, 1:-1, 1:-1]
    y_sides = padded[1:-1, 2:, 1:-1] + padded[1:-1, :-2, 1:-1]
    z_sides = padded[1:-1, 1:-1, 2:] + padded[1:-1, 1:-1, :-2]
    return x_sides + y_sides + z_sides


def _select_tree(material, table_ref):
    bits = [(material & (1 << b)) != 0 for b in range(3)]
    level = [table_ref[k] for k in range(8)]
    for bit in bits:
        level = [jnp.where(bit, level[k + 1], level[k]) for k in range(0, len(level), 2)]
    return level[0]


def _lookup_kernel(cond_table, drain_table, material_ref, cond_ref, drain_ref):
    material = material_ref[...]
    cond_ref[...] = _select_tree(material, cond_table)
    drain_ref[...] = _select_tree(material, drain_table)


def lookup_both(material, conductance, rock_heat_drain):
    planes = material.shape[0]
    block = (4,) + material.shape[1:]
    spec = pl.BlockSpec(block, lambda i: (i, 0, 0))
    smem = pl.BlockSpec(memory_space=pltpu.SMEM)
    out = jax.ShapeDtypeStruct(material.shape, jnp.float32)
    return pl.pallas_call(
        _lookup_kernel,
        grid=(planes // block[0],),
        in_specs=[smem, smem, spec],
        out_specs=[spec, spec],
        out_shape=[out, out],
    )(conductance, rock_heat_drain, material)


def on_device(
    prior_adjoint_iterate,
    material,
    probe_cell_index,
    misfit,
    ventilation_heat_loss,
    conductance,
    rock_heat_drain,
):
    adjoint = prior_adjoint_iterate[0]
    planes = adjoint.shape[0]
    across = adjoint.shape[1]
    depth = adjoint.shape[2]
    local_cell = probe_cell_index - lax.axis_index("space") * (planes * across * depth)
    source = (
        jnp.zeros((planes * across * depth,), jnp.float32)
        .at[local_cell]
        .add(misfit[0])
        .reshape(planes, across, depth)
    )
    seeded = adjoint + source
    halo = FINE_STEPS
    space_size = lax.axis_size("space")
    up = [(i, i + 1) for i in range(space_size - 1)]
    down = [(i + 1, i) for i in range(space_size - 1)]
    material_f = material.astype(jnp.float32)
    to_next = jnp.concatenate([seeded[-halo:], material_f[-halo:]], axis=0)
    to_prev = jnp.concatenate([seeded[:halo], material_f[:halo]], axis=0)
    from_prev = lax.ppermute(to_next, "space", up)
    from_next = lax.ppermute(to_prev, "space", down)
    current = jnp.concatenate([from_prev[:halo], seeded, from_next[:halo]], axis=0)
    material_ext = jnp.concatenate(
        [from_prev[halo:], material_f, from_next[halo:]], axis=0
    ).astype(jnp.int32)
    cond_ext, drain_ext = lookup_both(material_ext, conductance, rock_heat_drain)
    extended = planes + 2 * halo
    plane = lax.axis_index("space") * planes - halo + lax.iota(jnp.int32, extended)
    inside = (plane >= 0) & (plane < space_size * planes)
    cond_ext = jnp.where(inside[:, None, None], cond_ext, 0.0)
    losses_ext = drain_ext + ventilation_heat_loss[0]
    for sweep_index in range(FINE_STEPS):
        lo, hi = sweep_index, extended - sweep_index
        weighted = cond_ext[lo:hi] * current
        x_sides = weighted[2:] + weighted[:-2]
        inner = weighted[1:-1]
        padded = jnp.pad(inner, ((0, 0), (1, 1), (1, 1)))
        y_sides = padded[:, 2:, 1:-1] + padded[:, :-2, 1:-1]
        z_sides = padded[:, 1:-1, 2:] + padded[:, 1:-1, :-2]
        kept = current[1:-1]
        current = kept + ((x_sides + y_sides + z_sides) - 6.0 * inner) - losses_ext[lo + 1 : hi - 1] * kept
    cell_heat_drain = drain_ext[halo : halo + planes]
    coarse_baseline = coarsen(cell_heat_drain)
    coarse_decay_rate = jnp.exp(-FINE_STEPS * (coarse_baseline + ventilation_heat_loss[0]))
    coarse_old = coarsen(adjoint)
    correction = current - refine(coarse_decay_rate * coarse_old)
    reduced = coarsen(correction)
    tm_size = lax.axis_size("tm")
    is_last = lax.axis_index("tm") == tm_size - 1
    per_cell = jnp.exp(-FINE_STEPS * coarse_baseline)
    gain = jnp.exp(-FINE_STEPS * ventilation_heat_loss[0])
    top = coarse_decay_rate * coarse_old + reduced
    total = jnp.where(is_last, top, reduced)
    shape = total.shape
    rows = total.size // shape[-1]
    power = per_cell
    distance = 1
    while distance < tm_size:
        packed = jnp.concatenate(
            [total.reshape(rows, shape[-1]), jnp.broadcast_to(gain, (8, shape[-1]))], axis=0
        )
        arrived = shifted(packed, "tm", -distance)
        total = total + (power * gain) * arrived[:rows].reshape(shape)
        gain = gain * arrived[rows, 0]
        power = power * power
        distance *= 2
    decayed = jnp.where(is_last, coarse_decay_rate * coarse_old, total - reduced)
    adjoint_new = refine(decayed) + correction
    return adjoint_new[None]


def solution(mesh):
    in_specs = (
        P("tm", "space", None, None),
        P("space", None, None),
        P("space"),
        P("tm", "space"),
        P("tm"),
        P(),
        P(),
    )
    out_specs = P("tm", "space", None, None)
    return jax.shard_map(
        on_device, mesh=mesh, in_specs=in_specs, out_specs=out_specs, check_vma=False
    )
```

```python
import jax
import jax.numpy as jnp
from jax import lax
from jax.experimental import pallas as pl
from jax.experimental.pallas import tpu as pltpu
from jax.sharding import PartitionSpec as P

FINE_STEPS = 4


def padded_2(value, sides, width):
    for axis, dim in sides:
        size, length = (lax.axis_size(axis), value.shape[dim])
        up = [(i, (i + 1) % size) for i in range(size - 1)]
        down = [(j, i) for i, j in up]
        last = lax.slice_in_dim(value, length - width, length, axis=dim)
        initial = lax.slice_in_dim(value, 0, width, axis=dim)
        before = lax.ppermute(last, axis, up)
        after = lax.ppermute(initial, axis, down)
        value = jnp.concatenate([before, value, after], axis=dim)
    return value


def shifted(value, axis, steps):
    count = lax.axis_size(axis)
    initial, last = (max(0, -steps), min(count, count - steps))
    return lax.ppermute(value, axis, [(source, source + steps) for source in range(initial, last)])


def coarsen(field):
    split = field.reshape(field.shape[0] // 2, 2, field.shape[1] // 2, 2, field.shape[2])
    return 0.25 * (split[:, 0, :, 0] + split[:, 1, :, 0] + (split[:, 0, :, 1] + split[:, 1, :, 1]))


def refine(coarse):
    return jnp.repeat(jnp.repeat(coarse, 2, axis=0), 2, axis=1)


def neighbours(padded):
    x_sides = padded[2:, 1:-1, 1:-1] + padded[:-2, 1:-1, 1:-1]
    y_sides = padded[1:-1, 2:, 1:-1] + padded[1:-1, :-2, 1:-1]
    z_sides = padded[1:-1, 1:-1, 2:] + padded[1:-1, 1:-1, :-2]
    return x_sides + y_sides + z_sides


def _select_tree(material, table_ref):
    bits = [(material & (1 << b)) != 0 for b in range(3)]
    level = [table_ref[k] for k in range(8)]
    for bit in bits:
        level = [jnp.where(bit, level[k + 1], level[k]) for k in range(0, len(level), 2)]
    return level[0]


def _lookup_kernel(cond_table, drain_table, material_ref, cond_ref, drain_ref):
    material = material_ref[...]
    cond_ref[...] = _select_tree(material, cond_table)
    drain_ref[...] = _select_tree(material, drain_table)


def lookup_both(material, conductance, rock_heat_drain):
    planes = material.shape[0]
    block = (4,) + material.shape[1:]
    spec = pl.BlockSpec(block, lambda i: (i, 0, 0))
    smem = pl.BlockSpec(memory_space=pltpu.SMEM)
    out = jax.ShapeDtypeStruct(material.shape, jnp.float32)
    return pl.pallas_call(
        _lookup_kernel,
        grid=(planes // block[0],),
        in_specs=[smem, smem, spec],
        out_specs=[spec, spec],
        out_shape=[out, out],
    )(conductance, rock_heat_drain, material)


def pack(field, scalar):
    return jnp.concatenate([field, jnp.broadcast_to(scalar, (8, field.shape[-1]))], axis=0)


def grouped_scan(total, gain, per_cell, group):
    tm_size = lax.axis_size("tm")
    member = lax.axis_index("tm") % group
    rows = total.shape[0]
    block_b, block_e = total, gain
    suffix_b, suffix_e, suffix_p = total, gain, per_cell
    power = per_cell
    bit = 1
    while bit < group:
        pairs = [(i, i ^ bit) for i in range(tm_size)]
        arrived = lax.ppermute(pack(block_b, block_e), "tm", pairs)
        other_b, other_e = arrived[:rows], arrived[rows, 0]
        above = (member & bit) == 0
        suffix_b = jnp.where(above, suffix_b + (suffix_p * suffix_e) * other_b, suffix_b)
        suffix_p = jnp.where(above, suffix_p * power, suffix_p)
        suffix_e = jnp.where(above, suffix_e * other_e, suffix_e)
        block_b = jnp.where(
            above, block_b + (power * block_e) * other_b, other_b + (power * other_e) * block_b
        )
        block_e = block_e * other_e
        power = power * power
        bit *= 2
    part = rows // group
    chain_b = lax.dynamic_slice_in_dim(block_b, member * part, part, 0)
    chain_p = lax.dynamic_slice_in_dim(power, member * part, part, 0)
    pairs = [(i + group, i) for i in range(tm_size - group)]
    arrived = lax.ppermute(pack(chain_b, block_e), "tm", pairs)
    chain_b, chain_e = arrived[:part], arrived[part, 0]
    distance = group
    while distance < tm_size:
        pairs = [(i + distance, i) for i in range(tm_size - distance)]
        arrived = lax.ppermute(pack(chain_b, chain_e), "tm", pairs)
        chain_b = chain_b + (chain_p * chain_e) * arrived[:part]
        chain_e = chain_e * arrived[part, 0]
        chain_p = chain_p * chain_p
        distance *= 2
    piece = chain_b
    bit = 1
    while bit < group:
        pairs = [(i, i ^ bit) for i in range(tm_size)]
        other = lax.ppermute(piece, "tm", pairs)
        low = (member & bit) == 0
        piece = jnp.where(
            low, jnp.concatenate([piece, other], axis=0), jnp.concatenate([other, piece], axis=0)
        )
        bit *= 2
    return suffix_b + (suffix_p * suffix_e) * piece


def on_device(
    prior_adjoint_iterate,
    material,
    probe_cell_index,
    misfit,
    ventilation_heat_loss,
    conductance,
    rock_heat_drain,
):
    adjoint = prior_adjoint_iterate[0]
    planes = adjoint.shape[0]
    across = adjoint.shape[1]
    depth = adjoint.shape[2]
    local_cell = probe_cell_index - lax.axis_index("space") * (planes * across * depth)
    source = (
        jnp.zeros((planes * across * depth,), jnp.float32)
        .at[local_cell]
        .add(misfit[0])
        .reshape(planes, across, depth)
    )
    seeded = adjoint + source
    halo = FINE_STEPS
    space_size = lax.axis_size("space")
    up = [(i, i + 1) for i in range(space_size - 1)]
    down = [(i + 1, i) for i in range(space_size - 1)]
    material_f = material.astype(jnp.float32)
    to_next = jnp.concatenate([seeded[-halo:], material_f[-halo:]], axis=0)
    to_prev = jnp.concatenate([seeded[:halo], material_f[:halo]], axis=0)
    from_prev = lax.ppermute(to_next, "space", up)
    from_next = lax.ppermute(to_prev, "space", down)
    current = jnp.concatenate([from_prev[:halo], seeded, from_next[:halo]], axis=0)
    material_ext = jnp.concatenate(
        [from_prev[halo:], material_f, from_next[halo:]], axis=0
    ).astype(jnp.int32)
    cond_ext, drain_ext = lookup_both(material_ext, conductance, rock_heat_drain)
    extended = planes + 2 * halo
    plane = lax.axis_index("space") * planes - halo + lax.iota(jnp.int32, extended)
    inside = (plane >= 0) & (plane < space_size * planes)
    cond_ext = jnp.where(inside[:, None, None], cond_ext, 0.0)
    losses_ext = drain_ext + ventilation_heat_loss[0]
    for sweep_index in range(FINE_STEPS):
        lo, hi = sweep_index, extended - sweep_index
        weighted = cond_ext[lo:hi] * current
        x_sides = weighted[2:] + weighted[:-2]
        inner = weighted[1:-1]
        padded = jnp.pad(inner, ((0, 0), (1, 1), (1, 1)))
        y_sides = padded[:, 2:, 1:-1] + padded[:, :-2, 1:-1]
        z_sides = padded[:, 1:-1, 2:] + padded[:, 1:-1, :-2]
        kept = current[1:-1]
        current = kept + ((x_sides + y_sides + z_sides) - 6.0 * inner) - losses_ext[lo + 1 : hi - 1] * kept
    cell_heat_drain = drain_ext[halo : halo + planes]
    coarse_baseline = coarsen(cell_heat_drain)
    coarse_decay_rate = jnp.exp(-FINE_STEPS * (coarse_baseline + ventilation_heat_loss[0]))
    coarse_old = coarsen(adjoint)
    correction = current - refine(coarse_decay_rate * coarse_old)
    reduced = coarsen(correction)
    tm_size = lax.axis_size("tm")
    is_last = lax.axis_index("tm") == tm_size - 1
    per_cell = jnp.exp(-FINE_STEPS * coarse_baseline)
    gain = jnp.exp(-FINE_STEPS * ventilation_heat_loss[0])
    top = coarse_decay_rate * coarse_old + reduced
    total = jnp.where(is_last, top, reduced)
    shape = total.shape
    width = shape[-1]
    rows = total.size // width
    group = 4
    if tm_size % group == 0 and rows % group == 0 and tm_size > group:
        total = grouped_scan(total.reshape(rows, width), gain, per_cell.reshape(rows, width), group)
        total = total.reshape(shape)
    else:
        power = per_cell
        distance = 1
        while distance < tm_size:
            arrived = shifted(pack(total.reshape(rows, width), gain), "tm", -distance)
            total = total + (power * gain) * arrived[:rows].reshape(shape)
            gain = gain * arrived[rows, 0]
            power = power * power
            distance *= 2
    decayed = jnp.where(is_last, coarse_decay_rate * coarse_old, total - reduced)
    adjoint_new = refine(decayed) + correction
    return adjoint_new[None]


def solution(mesh):
    in_specs = (
        P("tm", "space", None, None),
        P("space", None, None),
        P("space"),
        P("tm", "space"),
        P("tm"),
        P(),
        P(),
    )
    out_specs = P("tm", "space", None, None)
    return jax.shard_map(
        on_device, mesh=mesh, in_specs=in_specs, out_specs=out_specs, check_vma=False
    )
```

```python
import jax
import jax.numpy as jnp
from jax import lax
from jax.experimental import pallas as pl
from jax.experimental.pallas import tpu as pltpu
from jax.sharding import PartitionSpec as P

FINE_STEPS = 4


def padded_2(value, sides, width):
    for axis, dim in sides:
        size, length = (lax.axis_size(axis), value.shape[dim])
        up = [(i, (i + 1) % size) for i in range(size - 1)]
        down = [(j, i) for i, j in up]
        last = lax.slice_in_dim(value, length - width, length, axis=dim)
        initial = lax.slice_in_dim(value, 0, width, axis=dim)
        before = lax.ppermute(last, axis, up)
        after = lax.ppermute(initial, axis, down)
        value = jnp.concatenate([before, value, after], axis=dim)
    return value


def shifted(value, axis, steps):
    count = lax.axis_size(axis)
    initial, last = (max(0, -steps), min(count, count - steps))
    return lax.ppermute(value, axis, [(source, source + steps) for source in range(initial, last)])


def coarsen(field):
    split = field.reshape(field.shape[0] // 2, 2, field.shape[1] // 2, 2, field.shape[2])
    return 0.25 * (split[:, 0, :, 0] + split[:, 1, :, 0] + (split[:, 0, :, 1] + split[:, 1, :, 1]))


def refine(coarse):
    return jnp.repeat(jnp.repeat(coarse, 2, axis=0), 2, axis=1)


def neighbours(padded):
    x_sides = padded[2:, 1:-1, 1:-1] + padded[:-2, 1:-1, 1:-1]
    y_sides = padded[1:-1, 2:, 1:-1] + padded[1:-1, :-2, 1:-1]
    z_sides = padded[1:-1, 1:-1, 2:] + padded[1:-1, 1:-1, :-2]
    return x_sides + y_sides + z_sides


def _select_tree(material, table_ref):
    bits = [(material & (1 << b)) != 0 for b in range(3)]
    level = [table_ref[k] for k in range(8)]
    for bit in bits:
        level = [jnp.where(bit, level[k + 1], level[k]) for k in range(0, len(level), 2)]
    return level[0]


def _lookup_kernel(cond_table, drain_table, material_ref, cond_ref, drain_ref):
    material = material_ref[...]
    cond_ref[...] = _select_tree(material, cond_table)
    drain_ref[...] = _select_tree(material, drain_table)


def lookup_both(material, conductance, rock_heat_drain):
    planes = material.shape[0]
    block = (4,) + material.shape[1:]
    spec = pl.BlockSpec(block, lambda i: (i, 0, 0))
    smem = pl.BlockSpec(memory_space=pltpu.SMEM)
    out = jax.ShapeDtypeStruct(material.shape, jnp.float32)
    return pl.pallas_call(
        _lookup_kernel,
        grid=(planes // block[0],),
        in_specs=[smem, smem, spec],
        out_specs=[spec, spec],
        out_shape=[out, out],
    )(conductance, rock_heat_drain, material)


def on_device(
    prior_adjoint_iterate,
    material,
    probe_cell_index,
    misfit,
    ventilation_heat_loss,
    conductance,
    rock_heat_drain,
):
    adjoint = prior_adjoint_iterate[0]
    planes = adjoint.shape[0]
    across = adjoint.shape[1]
    depth = adjoint.shape[2]
    local_cell = probe_cell_index - lax.axis_index("space") * (planes * across * depth)
    source = (
        jnp.zeros((planes * across * depth,), jnp.float32)
        .at[local_cell]
        .add(misfit[0])
        .reshape(planes, across, depth)
    )
    seeded = adjoint + source
    halo = FINE_STEPS
    space_size = lax.axis_size("space")
    up = [(i, i + 1) for i in range(space_size - 1)]
    down = [(i + 1, i) for i in range(space_size - 1)]
    material_f = material.astype(jnp.float32)
    material_prev = lax.ppermute(material_f[-halo:], "space", up)
    material_next = lax.ppermute(material_f[:halo], "space", down)
    seeded_prev = lax.ppermute(seeded[-halo:], "space", up)
    seeded_next = lax.ppermute(seeded[:halo], "space", down)
    cond_own, drain_own = lookup_both(material, conductance, rock_heat_drain)
    halo_material = jnp.concatenate([material_prev, material_next], axis=0).astype(jnp.int32)
    cond_halo, drain_halo = lookup_both(halo_material, conductance, rock_heat_drain)
    current = jnp.concatenate([seeded_prev, seeded, seeded_next], axis=0)
    cond_ext = jnp.concatenate([cond_halo[:halo], cond_own, cond_halo[halo:]], axis=0)
    drain_ext = jnp.concatenate([drain_halo[:halo], drain_own, drain_halo[halo:]], axis=0)
    extended = planes + 2 * halo
    plane = lax.axis_index("space") * planes - halo + lax.iota(jnp.int32, extended)
    inside = (plane >= 0) & (plane < space_size * planes)
    cond_ext = jnp.where(inside[:, None, None], cond_ext, 0.0)
    losses_ext = drain_ext + ventilation_heat_loss[0]
    for sweep_index in range(FINE_STEPS):
        lo, hi = sweep_index, extended - sweep_index
        weighted = cond_ext[lo:hi] * current
        x_sides = weighted[2:] + weighted[:-2]
        inner = weighted[1:-1]
        padded = jnp.pad(inner, ((0, 0), (1, 1), (1, 1)))
        y_sides = padded[:, 2:, 1:-1] + padded[:, :-2, 1:-1]
        z_sides = padded[:, 1:-1, 2:] + padded[:, 1:-1, :-2]
        kept = current[1:-1]
        current = kept + ((x_sides + y_sides + z_sides) - 6.0 * inner) - losses_ext[lo + 1 : hi - 1] * kept
    cell_heat_drain = drain_own
    coarse_baseline = coarsen(cell_heat_drain)
    coarse_decay_rate = jnp.exp(-FINE_STEPS * (coarse_baseline + ventilation_heat_loss[0]))
    coarse_old = coarsen(adjoint)
    correction = current - refine(coarse_decay_rate * coarse_old)
    reduced = coarsen(correction)
    tm_size = lax.axis_size("tm")
    is_last = lax.axis_index("tm") == tm_size - 1
    per_cell = jnp.exp(-FINE_STEPS * coarse_baseline)
    gain = jnp.exp(-FINE_STEPS * ventilation_heat_loss[0])
    top = coarse_decay_rate * coarse_old + reduced
    total = jnp.where(is_last, top, reduced)
    shape = total.shape
    rows = total.size // shape[-1]
    power = per_cell
    distance = 1
    while distance < tm_size:
        packed = jnp.concatenate(
            [total.reshape(rows, shape[-1]), jnp.broadcast_to(gain, (8, shape[-1]))], axis=0
        )
        arrived = shifted(packed, "tm", -distance)
        total = total + (power * gain) * arrived[:rows].reshape(shape)
        gain = gain * arrived[rows, 0]
        power = power * power
        distance *= 2
    decayed = jnp.where(is_last, coarse_decay_rate * coarse_old, total - reduced)
    adjoint_new = refine(decayed) + correction
    return adjoint_new[None]


def solution(mesh):
    in_specs = (
        P("tm", "space", None, None),
        P("space", None, None),
        P("space"),
        P("tm", "space"),
        P("tm"),
        P(),
        P(),
    )
    out_specs = P("tm", "space", None, None)
    return jax.shard_map(
        on_device, mesh=mesh, in_specs=in_specs, out_specs=out_specs, check_vma=False
    )
```

```python
import jax
import jax.numpy as jnp
from jax import lax
from jax.experimental import pallas as pl
from jax.experimental.pallas import tpu as pltpu
from jax.sharding import PartitionSpec as P

FINE_STEPS = 4


def padded_2(value, sides, width):
    for axis, dim in sides:
        size, length = (lax.axis_size(axis), value.shape[dim])
        up = [(i, (i + 1) % size) for i in range(size - 1)]
        down = [(j, i) for i, j in up]
        last = lax.slice_in_dim(value, length - width, length, axis=dim)
        initial = lax.slice_in_dim(value, 0, width, axis=dim)
        before = lax.ppermute(last, axis, up)
        after = lax.ppermute(initial, axis, down)
        value = jnp.concatenate([before, value, after], axis=dim)
    return value


def shifted(value, axis, steps):
    count = lax.axis_size(axis)
    initial, last = (max(0, -steps), min(count, count - steps))
    return lax.ppermute(value, axis, [(source, source + steps) for source in range(initial, last)])


def coarsen(field):
    split = field.reshape(field.shape[0] // 2, 2, field.shape[1] // 2, 2, field.shape[2])
    return 0.25 * (split[:, 0, :, 0] + split[:, 1, :, 0] + (split[:, 0, :, 1] + split[:, 1, :, 1]))


def refine(coarse):
    return jnp.repeat(jnp.repeat(coarse, 2, axis=0), 2, axis=1)


def neighbours(padded):
    x_sides = padded[2:, 1:-1, 1:-1] + padded[:-2, 1:-1, 1:-1]
    y_sides = padded[1:-1, 2:, 1:-1] + padded[1:-1, :-2, 1:-1]
    z_sides = padded[1:-1, 1:-1, 2:] + padded[1:-1, 1:-1, :-2]
    return x_sides + y_sides + z_sides


def _select_tree(material, table_ref):
    bits = [(material & (1 << b)) != 0 for b in range(3)]
    level = [table_ref[k] for k in range(8)]
    for bit in bits:
        level = [jnp.where(bit, level[k + 1], level[k]) for k in range(0, len(level), 2)]
    return level[0]


def _lookup_kernel(cond_table, drain_table, material_ref, cond_ref, drain_ref):
    material = material_ref[...]
    cond_ref[...] = _select_tree(material, cond_table)
    drain_ref[...] = _select_tree(material, drain_table)


def lookup_both(material, conductance, rock_heat_drain):
    planes = material.shape[0]
    block = (4,) + material.shape[1:]
    spec = pl.BlockSpec(block, lambda i: (i, 0, 0))
    smem = pl.BlockSpec(memory_space=pltpu.SMEM)
    out = jax.ShapeDtypeStruct(material.shape, jnp.float32)
    return pl.pallas_call(
        _lookup_kernel,
        grid=(planes // block[0],),
        in_specs=[smem, smem, spec],
        out_specs=[spec, spec],
        out_shape=[out, out],
    )(conductance, rock_heat_drain, material)


def pack(field, scalar):
    return jnp.concatenate([field, jnp.broadcast_to(scalar, (8, field.shape[-1]))], axis=0)


def fine_steps(current, cond, losses):
    planes = current.shape[0]
    for sweep_index in range(FINE_STEPS):
        lo, hi = sweep_index, planes - sweep_index
        weighted = cond[lo:hi] * current
        x_sides = weighted[2:] + weighted[:-2]
        inner = weighted[1:-1]
        padded = jnp.pad(inner, ((0, 0), (1, 1), (1, 1)))
        y_sides = padded[:, 2:, 1:-1] + padded[:, :-2, 1:-1]
        z_sides = padded[:, 1:-1, 2:] + padded[:, 1:-1, :-2]
        kept = current[1:-1]
        current = kept + ((x_sides + y_sides + z_sides) - 6.0 * inner) - losses[lo + 1 : hi - 1] * kept
    return current


def on_device(
    prior_adjoint_iterate,
    material,
    probe_cell_index,
    misfit,
    ventilation_heat_loss,
    conductance,
    rock_heat_drain,
):
    adjoint = prior_adjoint_iterate[0]
    planes = adjoint.shape[0]
    across = adjoint.shape[1]
    depth = adjoint.shape[2]
    local_cell = probe_cell_index - lax.axis_index("space") * (planes * across * depth)
    source = (
        jnp.zeros((planes * across * depth,), jnp.float32)
        .at[local_cell]
        .add(misfit[0])
        .reshape(planes, across, depth)
    )
    seeded = adjoint + source
    halo = FINE_STEPS
    space_size = lax.axis_size("space")
    up = [(i, i + 1) for i in range(space_size - 1)]
    down = [(i + 1, i) for i in range(space_size - 1)]
    material_f = material.astype(jnp.float32)
    material_prev = lax.ppermute(material_f[-halo:], "space", up)
    material_next = lax.ppermute(material_f[:halo], "space", down)
    seeded_prev = lax.ppermute(seeded[-halo:], "space", up)
    seeded_next = lax.ppermute(seeded[:halo], "space", down)
    cond_own, drain_own = lookup_both(material, conductance, rock_heat_drain)
    halo_material = jnp.concatenate([material_prev, material_next], axis=0).astype(jnp.int32)
    cond_halo, drain_halo = lookup_both(halo_material, conductance, rock_heat_drain)
    current = jnp.concatenate([seeded_prev, seeded, seeded_next], axis=0)
    cond_ext = jnp.concatenate([cond_halo[:halo], cond_own, cond_halo[halo:]], axis=0)
    drain_ext = jnp.concatenate([drain_halo[:halo], drain_own, drain_halo[halo:]], axis=0)
    extended = planes + 2 * halo
    plane = lax.axis_index("space") * planes - halo + lax.iota(jnp.int32, extended)
    inside = (plane >= 0) & (plane < space_size * planes)
    cond_ext = jnp.where(inside[:, None, None], cond_ext, 0.0)
    losses_ext = drain_ext + ventilation_heat_loss[0]
    losses_own = drain_own + ventilation_heat_loss[0]
    middle = fine_steps(seeded, cond_own, losses_own)
    coarse_baseline = coarsen(drain_own)
    coarse_decay_rate = jnp.exp(-FINE_STEPS * (coarse_baseline + ventilation_heat_loss[0]))
    coarse_old = coarsen(adjoint)
    decayed_old = coarse_decay_rate * coarse_old
    edge = halo // 2
    coarse_planes = coarse_old.shape[0]
    inner = slice(edge, coarse_planes - edge)
    correction_mid = middle - refine(decayed_old[inner])
    reduced_mid = coarsen(correction_mid)
    decayed_edge = jnp.concatenate([decayed_old[:edge], decayed_old[-edge:]], axis=0)
    tm_size = lax.axis_size("tm")
    is_last = lax.axis_index("tm") == tm_size - 1
    per_cell = jnp.exp(-FINE_STEPS * coarse_baseline)
    gain = jnp.exp(-FINE_STEPS * ventilation_heat_loss[0])
    total_mid = jnp.where(is_last, decayed_old[inner] + reduced_mid, reduced_mid)
    power_mid = per_cell[inner]
    power_edge = jnp.concatenate([per_cell[:edge], per_cell[-edge:]], axis=0)
    shape = total_mid.shape
    width = shape[-1]
    rows = total_mid.size // width
    gains = []
    distance = 1
    while distance < tm_size:
        gains.append(gain)
        arrived = shifted(pack(total_mid.reshape(rows, width), gain), "tm", -distance)
        total_mid = total_mid + (power_mid * gain) * arrived[:rows].reshape(shape)
        gain = gain * arrived[rows, 0]
        power_mid = power_mid * power_mid
        distance *= 2
    current, cond_ext, losses_ext, total_mid = lax.optimization_barrier(
        (current, cond_ext, losses_ext, total_mid)
    )
    low = fine_steps(current[: 3 * halo], cond_ext[: 3 * halo], losses_ext[: 3 * halo])
    high = fine_steps(current[-3 * halo :], cond_ext[-3 * halo :], losses_ext[-3 * halo :])
    correction_low = low - refine(decayed_old[:edge])
    correction_high = high - refine(decayed_old[-edge:])
    reduced_edge = jnp.concatenate([coarsen(correction_low), coarsen(correction_high)], axis=0)
    total_edge = jnp.where(is_last, decayed_edge + reduced_edge, reduced_edge)
    distance = 1
    for own_gain in gains:
        arrived = shifted(total_edge, "tm", -distance)
        total_edge = total_edge + (power_edge * own_gain) * arrived
        power_edge = power_edge * power_edge
        distance *= 2
    total = jnp.concatenate([total_edge[:edge], total_mid, total_edge[edge:]], axis=0)
    reduced = jnp.concatenate([reduced_edge[:edge], reduced_mid, reduced_edge[edge:]], axis=0)
    correction = jnp.concatenate([correction_low, correction_mid, correction_high], axis=0)
    decayed = jnp.where(is_last, decayed_old, total - reduced)
    adjoint_new = refine(decayed) + correction
    return adjoint_new[None]


def solution(mesh):
    in_specs = (
        P("tm", "space", None, None),
        P("space", None, None),
        P("space"),
        P("tm", "space"),
        P("tm"),
        P(),
        P(),
    )
    out_specs = P("tm", "space", None, None)
    return jax.shard_map(
        on_device, mesh=mesh, in_specs=in_specs, out_specs=out_specs, check_vma=False
    )
```

```python
import jax
import jax.numpy as jnp
from jax import lax
from jax.experimental import pallas as pl
from jax.experimental.pallas import tpu as pltpu
from jax.sharding import PartitionSpec as P

FINE_STEPS = 4


def padded_2(value, sides, width):
    for axis, dim in sides:
        size, length = (lax.axis_size(axis), value.shape[dim])
        up = [(i, (i + 1) % size) for i in range(size - 1)]
        down = [(j, i) for i, j in up]
        last = lax.slice_in_dim(value, length - width, length, axis=dim)
        initial = lax.slice_in_dim(value, 0, width, axis=dim)
        before = lax.ppermute(last, axis, up)
        after = lax.ppermute(initial, axis, down)
        value = jnp.concatenate([before, value, after], axis=dim)
    return value


def shifted(value, axis, steps):
    count = lax.axis_size(axis)
    initial, last = (max(0, -steps), min(count, count - steps))
    return lax.ppermute(value, axis, [(source, source + steps) for source in range(initial, last)])


def coarsen(field):
    split = field.reshape(field.shape[0] // 2, 2, field.shape[1] // 2, 2, field.shape[2])
    return 0.25 * (split[:, 0, :, 0] + split[:, 1, :, 0] + (split[:, 0, :, 1] + split[:, 1, :, 1]))


def refine(coarse):
    return jnp.repeat(jnp.repeat(coarse, 2, axis=0), 2, axis=1)


def neighbours(padded):
    x_sides = padded[2:, 1:-1, 1:-1] + padded[:-2, 1:-1, 1:-1]
    y_sides = padded[1:-1, 2:, 1:-1] + padded[1:-1, :-2, 1:-1]
    z_sides = padded[1:-1, 1:-1, 2:] + padded[1:-1, 1:-1, :-2]
    return x_sides + y_sides + z_sides


def _select_tree(material, table_ref):
    bits = [(material & (1 << b)) != 0 for b in range(3)]
    level = [table_ref[k] for k in range(8)]
    for bit in bits:
        level = [jnp.where(bit, level[k + 1], level[k]) for k in range(0, len(level), 2)]
    return level[0]


def _lookup_kernel(cond_table, drain_table, material_ref, cond_ref, drain_ref):
    material = material_ref[...]
    cond_ref[...] = _select_tree(material, cond_table)
    drain_ref[...] = _select_tree(material, drain_table)


def lookup_both(material, conductance, rock_heat_drain):
    planes = material.shape[0]
    block = (4,) + material.shape[1:]
    spec = pl.BlockSpec(block, lambda i: (i, 0, 0))
    smem = pl.BlockSpec(memory_space=pltpu.SMEM)
    out = jax.ShapeDtypeStruct(material.shape, jnp.float32)
    return pl.pallas_call(
        _lookup_kernel,
        grid=(planes // block[0],),
        in_specs=[smem, smem, spec],
        out_specs=[spec, spec],
        out_shape=[out, out],
    )(conductance, rock_heat_drain, material)


def on_device(
    prior_adjoint_iterate,
    material,
    probe_cell_index,
    misfit,
    ventilation_heat_loss,
    conductance,
    rock_heat_drain,
):
    adjoint = prior_adjoint_iterate[0]
    planes = adjoint.shape[0]
    across = adjoint.shape[1]
    depth = adjoint.shape[2]
    local_cell = probe_cell_index - lax.axis_index("space") * (planes * across * depth)
    source = (
        jnp.zeros((planes * across * depth,), jnp.float32)
        .at[local_cell]
        .add(misfit[0])
        .reshape(planes, across, depth)
    )
    seeded = adjoint + source
    halo = FINE_STEPS
    space_size = lax.axis_size("space")
    up = [(i, i + 1) for i in range(space_size - 1)]
    down = [(i + 1, i) for i in range(space_size - 1)]
    material_f = material.astype(jnp.float32)
    material_prev = lax.ppermute(material_f[-halo:], "space", up)
    material_next = lax.ppermute(material_f[:halo], "space", down)
    seeded_prev = lax.ppermute(seeded[-halo:], "space", up)
    seeded_next = lax.ppermute(seeded[:halo], "space", down)
    cond_own, drain_own = lookup_both(material, conductance, rock_heat_drain)
    halo_material = jnp.concatenate([material_prev, material_next], axis=0).astype(jnp.int32)
    cond_halo, drain_halo = lookup_both(halo_material, conductance, rock_heat_drain)
    current = jnp.concatenate([seeded_prev, seeded, seeded_next], axis=0)
    cond_ext = jnp.concatenate([cond_halo[:halo], cond_own, cond_halo[halo:]], axis=0)
    drain_ext = jnp.concatenate([drain_halo[:halo], drain_own, drain_halo[halo:]], axis=0)
    extended = planes + 2 * halo
    plane = lax.axis_index("space") * planes - halo + lax.iota(jnp.int32, extended)
    inside = (plane >= 0) & (plane < space_size * planes)
    cond_ext = jnp.where(inside[:, None, None], cond_ext, 0.0)
    losses_ext = drain_ext + ventilation_heat_loss[0]
    for sweep_index in range(FINE_STEPS):
        lo, hi = sweep_index, extended - sweep_index
        weighted = cond_ext[lo:hi] * current
        x_sides = weighted[2:] + weighted[:-2]
        inner = weighted[1:-1]
        padded = jnp.pad(inner, ((0, 0), (1, 1), (1, 1)))
        y_sides = padded[:, 2:, 1:-1] + padded[:, :-2, 1:-1]
        z_sides = padded[:, 1:-1, 2:] + padded[:, 1:-1, :-2]
        kept = current[1:-1]
        current = kept + ((x_sides + y_sides + z_sides) - 6.0 * inner) - losses_ext[lo + 1 : hi - 1] * kept
    cell_heat_drain = drain_own
    coarse_baseline = coarsen(cell_heat_drain)
    coarse_decay_rate = jnp.exp(-FINE_STEPS * (coarse_baseline + ventilation_heat_loss[0]))
    coarse_old = coarsen(adjoint)
    correction = current - refine(coarse_decay_rate * coarse_old)
    reduced = coarsen(correction)
    tm_size = lax.axis_size("tm")
    is_last = lax.axis_index("tm") == tm_size - 1
    per_cell = jnp.exp(-FINE_STEPS * coarse_baseline)
    gain = jnp.exp(-FINE_STEPS * ventilation_heat_loss[0])
    top = coarse_decay_rate * coarse_old + reduced
    total = jnp.where(is_last, top, reduced)
    shape = total.shape
    width = shape[-1]
    rows = total.size // width
    packed = jnp.concatenate(
        [total.reshape(rows, width), jnp.broadcast_to(gain, (8, width))], axis=0
    )
    power = jnp.concatenate([per_cell.reshape(rows, width), jnp.ones((8, width), jnp.float32)], axis=0)
    is_field = lax.broadcasted_iota(jnp.int32, packed.shape, 0) < rows
    distance = 1
    while distance < tm_size:
        arrived = shifted(packed, "tm", -distance)
        own_gain = packed[rows, 0]
        packed = jnp.where(is_field, packed + (power * own_gain) * arrived, packed * arrived)
        power = power * power
        distance *= 2
    total = packed[:rows].reshape(shape)
    decayed = jnp.where(is_last, coarse_decay_rate * coarse_old, total - reduced)
    adjoint_new = refine(decayed) + correction
    return adjoint_new[None]


def solution(mesh):
    in_specs = (
        P("tm", "space", None, None),
        P("space", None, None),
        P("space"),
        P("tm", "space"),
        P("tm"),
        P(),
        P(),
    )
    out_specs = P("tm", "space", None, None)
    return jax.shard_map(
        on_device, mesh=mesh, in_specs=in_specs, out_specs=out_specs, check_vma=False
    )
```

```python
import jax
import jax.numpy as jnp
from jax import lax
from jax.experimental import pallas as pl
from jax.experimental.pallas import tpu as pltpu
from jax.sharding import PartitionSpec as P

FINE_STEPS = 4


def shifted(value, axis, steps):
    count = lax.axis_size(axis)
    initial, last = (max(0, -steps), min(count, count - steps))
    return lax.ppermute(value, axis, [(source, source + steps) for source in range(initial, last)])


def coarsen(field):
    split = field.reshape(field.shape[0] // 2, 2, field.shape[1] // 2, 2, field.shape[2])
    return 0.25 * (split[:, 0, :, 0] + split[:, 1, :, 0] + (split[:, 0, :, 1] + split[:, 1, :, 1]))


def refine(coarse):
    return jnp.repeat(jnp.repeat(coarse, 2, axis=0), 2, axis=1)


def _select_tree(material, table_ref):
    bits = [(material & (1 << b)) != 0 for b in range(3)]
    level = [table_ref[k] for k in range(8)]
    for bit in bits:
        level = [jnp.where(bit, level[k + 1], level[k]) for k in range(0, len(level), 2)]
    return level[0]


def _lookup_kernel(cond_table, drain_table, material_ref, cond_ref, drain_ref):
    material = material_ref[...]
    cond_ref[...] = _select_tree(material, cond_table)
    drain_ref[...] = _select_tree(material, drain_table)


def lookup_both(material, conductance, rock_heat_drain):
    planes = material.shape[0]
    block = (4,) + material.shape[1:]
    spec = pl.BlockSpec(block, lambda i: (i, 0, 0))
    smem = pl.BlockSpec(memory_space=pltpu.SMEM)
    out = jax.ShapeDtypeStruct(material.shape, jnp.float32)
    return pl.pallas_call(
        _lookup_kernel,
        grid=(planes // block[0],),
        in_specs=[smem, smem, spec],
        out_specs=[spec, spec],
        out_shape=[out, out],
    )(conductance, rock_heat_drain, material)


def on_device(
    prior_adjoint_iterate,
    material,
    probe_cell_index,
    misfit,
    ventilation_heat_loss,
    conductance,
    rock_heat_drain,
):
    adjoint = prior_adjoint_iterate[0]
    planes = adjoint.shape[0]
    across = adjoint.shape[1]
    depth = adjoint.shape[2]
    local_cell = probe_cell_index - lax.axis_index("space") * (planes * across * depth)
    source = (
        jnp.zeros((planes * across * depth,), jnp.float32)
        .at[local_cell]
        .add(misfit[0])
        .reshape(planes, across, depth)
    )
    seeded = adjoint + source
    halo = FINE_STEPS
    space_size = lax.axis_size("space")
    up = [(i, i + 1) for i in range(space_size - 1)]
    down = [(i + 1, i) for i in range(space_size - 1)]
    material_f = material.astype(jnp.float32)
    material_prev = lax.ppermute(material_f[-halo:], "space", up)
    cond_own, drain_own = lookup_both(material, conductance, rock_heat_drain)
    material_low, cond_own, drain_own = lax.optimization_barrier(
        (material_f[:halo], cond_own, drain_own)
    )
    material_next = lax.ppermute(material_low, "space", down)
    seeded_prev = lax.ppermute(seeded[-halo:], "space", up)
    coarse_baseline = coarsen(drain_own)
    coarse_decay_rate = jnp.exp(-FINE_STEPS * (coarse_baseline + ventilation_heat_loss[0]))
    coarse_old = coarsen(adjoint)
    seeded_low, coarse_baseline, coarse_decay_rate, coarse_old = lax.optimization_barrier(
        (seeded[:halo], coarse_baseline, coarse_decay_rate, coarse_old)
    )
    seeded_next = lax.ppermute(seeded_low, "space", down)
    halo_material = jnp.concatenate([material_prev, material_next], axis=0).astype(jnp.int32)
    cond_halo, drain_halo = lookup_both(halo_material, conductance, rock_heat_drain)
    current = jnp.concatenate([seeded_prev, seeded, seeded_next], axis=0)
    cond_ext = jnp.concatenate([cond_halo[:halo], cond_own, cond_halo[halo:]], axis=0)
    drain_ext = jnp.concatenate([drain_halo[:halo], drain_own, drain_halo[halo:]], axis=0)
    extended = planes + 2 * halo
    plane = lax.axis_index("space") * planes - halo + lax.iota(jnp.int32, extended)
    inside = (plane >= 0) & (plane < space_size * planes)
    cond_ext = jnp.where(inside[:, None, None], cond_ext, 0.0)
    losses_ext = drain_ext + ventilation_heat_loss[0]
    for sweep_index in range(FINE_STEPS):
        lo, hi = sweep_index, extended - sweep_index
        weighted = cond_ext[lo:hi] * current
        x_sides = weighted[2:] + weighted[:-2]
        inner = weighted[1:-1]
        padded = jnp.pad(inner, ((0, 0), (1, 1), (1, 1)))
        y_sides = padded[:, 2:, 1:-1] + padded[:, :-2, 1:-1]
        z_sides = padded[:, 1:-1, 2:] + padded[:, 1:-1, :-2]
        kept = current[1:-1]
        current = kept + ((x_sides + y_sides + z_sides) - 6.0 * inner) - losses_ext[lo + 1 : hi - 1] * kept
    correction = current - refine(coarse_decay_rate * coarse_old)
    reduced = coarsen(correction)
    tm_size = lax.axis_size("tm")
    is_last = lax.axis_index("tm") == tm_size - 1
    per_cell = jnp.exp(-FINE_STEPS * coarse_baseline)
    gain = jnp.exp(-FINE_STEPS * ventilation_heat_loss[0])
    top = coarse_decay_rate * coarse_old + reduced
    total = jnp.where(is_last, top, reduced)
    shape = total.shape
    width = shape[-1]
    rows = total.size // width
    packed = jnp.concatenate(
        [total.reshape(rows, width), jnp.broadcast_to(gain, (8, width))], axis=0
    )
    power = jnp.concatenate([per_cell.reshape(rows, width), jnp.ones((8, width), jnp.float32)], axis=0)
    is_field = lax.broadcasted_iota(jnp.int32, packed.shape, 0) < rows
    distance = 1
    while distance < tm_size:
        arrived = shifted(packed, "tm", -distance)
        own_gain = packed[rows, 0]
        packed = jnp.where(is_field, packed + (power * own_gain) * arrived, packed * arrived)
        power = power * power
        distance *= 2
    total = packed[:rows].reshape(shape)
    decayed = jnp.where(is_last, coarse_decay_rate * coarse_old, total - reduced)
    adjoint_new = refine(decayed) + correction
    return adjoint_new[None]


def solution(mesh):
    in_specs = (
        P("tm", "space", None, None),
        P("space", None, None),
        P("space"),
        P("tm", "space"),
        P("tm"),
        P(),
        P(),
    )
    out_specs = P("tm", "space", None, None)

    return jax.shard_map(
        on_device, mesh=mesh, in_specs=in_specs, out_specs=out_specs, check_vma=False
    )
```

```python
import jax
import jax.numpy as jnp
from jax import lax
from jax.experimental import pallas as pl
from jax.experimental.pallas import tpu as pltpu
from jax.sharding import PartitionSpec as P

FINE_STEPS = 4


def padded_2(value, sides, width):
    for axis, dim in sides:
        size, length = (lax.axis_size(axis), value.shape[dim])
        up = [(i, (i + 1) % size) for i in range(size - 1)]
        down = [(j, i) for i, j in up]
        last = lax.slice_in_dim(value, length - width, length, axis=dim)
        initial = lax.slice_in_dim(value, 0, width, axis=dim)
        before = lax.ppermute(last, axis, up)
        after = lax.ppermute(initial, axis, down)
        value = jnp.concatenate([before, value, after], axis=dim)
    return value


def shifted(value, axis, steps):
    count = lax.axis_size(axis)
    initial, last = (max(0, -steps), min(count, count - steps))
    return lax.ppermute(value, axis, [(source, source + steps) for source in range(initial, last)])


def coarsen(field):
    split = field.reshape(field.shape[0] // 2, 2, field.shape[1] // 2, 2, field.shape[2])
    return 0.25 * (split[:, 0, :, 0] + split[:, 1, :, 0] + (split[:, 0, :, 1] + split[:, 1, :, 1]))


def refine(coarse):
    return jnp.repeat(jnp.repeat(coarse, 2, axis=0), 2, axis=1)


def neighbours(padded):
    x_sides = padded[2:, 1:-1, 1:-1] + padded[:-2, 1:-1, 1:-1]
    y_sides = padded[1:-1, 2:, 1:-1] + padded[1:-1, :-2, 1:-1]
    z_sides = padded[1:-1, 1:-1, 2:] + padded[1:-1, 1:-1, :-2]
    return x_sides + y_sides + z_sides


def _select_tree(material, table_ref):
    bits = [(material & (1 << b)) != 0 for b in range(3)]
    level = [table_ref[k] for k in range(8)]
    for bit in bits:
        level = [jnp.where(bit, level[k + 1], level[k]) for k in range(0, len(level), 2)]
    return level[0]


def _lookup_kernel(cond_table, drain_table, material_ref, cond_ref, drain_ref):
    material = material_ref[...]
    cond_ref[...] = _select_tree(material, cond_table)
    drain_ref[...] = _select_tree(material, drain_table)


def lookup_both(material, conductance, rock_heat_drain):
    planes = material.shape[0]
    block = material.shape
    spec = pl.BlockSpec(block, lambda i: (i, 0, 0))
    smem = pl.BlockSpec(memory_space=pltpu.SMEM)
    out = jax.ShapeDtypeStruct(material.shape, jnp.float32)
    return pl.pallas_call(
        _lookup_kernel,
        grid=(planes // block[0],),
        in_specs=[smem, smem, spec],
        out_specs=[spec, spec],
        out_shape=[out, out],
    )(conductance, rock_heat_drain, material)


def on_device(
    prior_adjoint_iterate,
    material,
    probe_cell_index,
    misfit,
    ventilation_heat_loss,
    conductance,
    rock_heat_drain,
):
    adjoint = prior_adjoint_iterate[0]
    planes = adjoint.shape[0]
    across = adjoint.shape[1]
    depth = adjoint.shape[2]
    local_cell = probe_cell_index - lax.axis_index("space") * (planes * across * depth)
    source = (
        jnp.zeros((planes * across * depth,), jnp.float32)
        .at[local_cell]
        .add(misfit[0])
        .reshape(planes, across, depth)
    )
    seeded = adjoint + source
    halo = FINE_STEPS
    space_size = lax.axis_size("space")
    up = [(i, i + 1) for i in range(space_size - 1)]
    down = [(i + 1, i) for i in range(space_size - 1)]
    material_f = material.astype(jnp.float32)
    material_prev = lax.ppermute(material_f[-halo:], "space", up)
    material_next = lax.ppermute(material_f[:halo], "space", down)
    seeded_prev = lax.ppermute(seeded[-halo:], "space", up)
    seeded_next = lax.ppermute(seeded[:halo], "space", down)
    cond_own, drain_own = lookup_both(material, conductance, rock_heat_drain)
    halo_material = jnp.concatenate([material_prev, material_next], axis=0).astype(jnp.int32)
    cond_halo, drain_halo = lookup_both(halo_material, conductance, rock_heat_drain)
    current = jnp.concatenate([seeded_prev, seeded, seeded_next], axis=0)
    cond_ext = jnp.concatenate([cond_halo[:halo], cond_own, cond_halo[halo:]], axis=0)
    drain_ext = jnp.concatenate([drain_halo[:halo], drain_own, drain_halo[halo:]], axis=0)
    extended = planes + 2 * halo
    plane = lax.axis_index("space") * planes - halo + lax.iota(jnp.int32, extended)
    inside = (plane >= 0) & (plane < space_size * planes)
    cond_ext = jnp.where(inside[:, None, None], cond_ext, 0.0)
    losses_ext = drain_ext + ventilation_heat_loss[0]
    for sweep_index in range(FINE_STEPS):
        lo, hi = sweep_index, extended - sweep_index
        weighted = cond_ext[lo:hi] * current
        x_sides = weighted[2:] + weighted[:-2]
        inner = weighted[1:-1]
        padded = jnp.pad(inner, ((0, 0), (1, 1), (1, 1)))
        y_sides = padded[:, 2:, 1:-1] + padded[:, :-2, 1:-1]
        z_sides = padded[:, 1:-1, 2:] + padded[:, 1:-1, :-2]
        kept = current[1:-1]
        current = kept + ((x_sides + y_sides + z_sides) - 6.0 * inner) - losses_ext[lo + 1 : hi - 1] * kept
    cell_heat_drain = drain_own
    coarse_baseline = coarsen(cell_heat_drain)
    coarse_decay_rate = jnp.exp(-FINE_STEPS * (coarse_baseline + ventilation_heat_loss[0]))
    coarse_old = coarsen(adjoint)
    correction = current - refine(coarse_decay_rate * coarse_old)
    reduced = coarsen(correction)
    tm_size = lax.axis_size("tm")
    is_last = lax.axis_index("tm") == tm_size - 1
    per_cell = jnp.exp(-FINE_STEPS * coarse_baseline)
    gain = jnp.exp(-FINE_STEPS * ventilation_heat_loss[0])
    top = coarse_decay_rate * coarse_old + reduced
    total = jnp.where(is_last, top, reduced)
    shape = total.shape
    width = shape[-1]
    rows = total.size // width
    packed = jnp.concatenate(
        [total.reshape(rows, width), jnp.broadcast_to(gain, (8, width))], axis=0
    )
    power = jnp.concatenate([per_cell.reshape(rows, width), jnp.ones((8, width), jnp.float32)], axis=0)
    is_field = lax.broadcasted_iota(jnp.int32, packed.shape, 0) < rows
    distance = 1
    while distance < tm_size:
        arrived = shifted(packed, "tm", -distance)
        own_gain = packed[rows, 0]
        packed = jnp.where(is_field, packed + (power * own_gain) * arrived, packed * arrived)
        power = power * power
        distance *= 2
    total = packed[:rows].reshape(shape)
    decayed = jnp.where(is_last, coarse_decay_rate * coarse_old, total - reduced)
    adjoint_new = refine(decayed) + correction
    return adjoint_new[None]


def solution(mesh):
    in_specs = (
        P("tm", "space", None, None),
        P("space", None, None),
        P("space"),
        P("tm", "space"),
        P("tm"),
        P(),
        P(),
    )
    out_specs = P("tm", "space", None, None)
    return jax.shard_map(
        on_device, mesh=mesh, in_specs=in_specs, out_specs=out_specs, check_vma=False
    )
```

```python
import jax
import jax.numpy as jnp
from jax import lax
from jax.experimental import pallas as pl
from jax.experimental.pallas import tpu as pltpu
from jax.sharding import PartitionSpec as P

FINE_STEPS = 4


def padded_2(value, sides, width):
    for axis, dim in sides:
        size, length = (lax.axis_size(axis), value.shape[dim])
        up = [(i, (i + 1) % size) for i in range(size - 1)]
        down = [(j, i) for i, j in up]
        last = lax.slice_in_dim(value, length - width, length, axis=dim)
        initial = lax.slice_in_dim(value, 0, width, axis=dim)
        before = lax.ppermute(last, axis, up)
        after = lax.ppermute(initial, axis, down)
        value = jnp.concatenate([before, value, after], axis=dim)
    return value


def shifted(value, axis, steps):
    count = lax.axis_size(axis)
    initial, last = (max(0, -steps), min(count, count - steps))
    return lax.ppermute(value, axis, [(source, source + steps) for source in range(initial, last)])


def coarsen(field):
    split = field.reshape(field.shape[0] // 2, 2, field.shape[1] // 2, 2, field.shape[2])
    return 0.25 * (split[:, 0, :, 0] + split[:, 1, :, 0] + (split[:, 0, :, 1] + split[:, 1, :, 1]))


def refine(coarse):
    return jnp.repeat(jnp.repeat(coarse, 2, axis=0), 2, axis=1)


def neighbours(padded):
    x_sides = padded[2:, 1:-1, 1:-1] + padded[:-2, 1:-1, 1:-1]
    y_sides = padded[1:-1, 2:, 1:-1] + padded[1:-1, :-2, 1:-1]
    z_sides = padded[1:-1, 1:-1, 2:] + padded[1:-1, 1:-1, :-2]
    return x_sides + y_sides + z_sides


def _select_tree(material, table_ref):
    bits = [(material & (1 << b)) != 0 for b in range(3)]
    level = [table_ref[k] for k in range(8)]
    for bit in bits:
        level = [jnp.where(bit, level[k + 1], level[k]) for k in range(0, len(level), 2)]
    return level[0]


def _lookup_kernel(cond_table, drain_table, material_ref, cond_ref, drain_ref):
    material = material_ref[...]
    cond_ref[...] = _select_tree(material, cond_table)
    drain_ref[...] = _select_tree(material, drain_table)


def lookup_both(material, conductance, rock_heat_drain):
    planes = material.shape[0]
    block = material.shape
    spec = pl.BlockSpec(block, lambda i: (i, 0, 0))
    smem = pl.BlockSpec(memory_space=pltpu.SMEM)
    out = jax.ShapeDtypeStruct(material.shape, jnp.float32)
    return pl.pallas_call(
        _lookup_kernel,
        grid=(planes // block[0],),
        in_specs=[smem, smem, spec],
        out_specs=[spec, spec],
        out_shape=[out, out],
    )(conductance, rock_heat_drain, material)


def on_device(
    prior_adjoint_iterate,
    material,
    probe_cell_index,
    misfit,
    ventilation_heat_loss,
    conductance,
    rock_heat_drain,
):
    adjoint = prior_adjoint_iterate[0]
    planes = adjoint.shape[0]
    across = adjoint.shape[1]
    depth = adjoint.shape[2]
    local_cell = probe_cell_index - lax.axis_index("space") * (planes * across * depth)
    source = (
        jnp.zeros((planes * across * depth,), jnp.float32)
        .at[local_cell]
        .add(misfit[0])
        .reshape(planes, across, depth)
    )
    seeded = adjoint + source
    halo = FINE_STEPS
    space_size = lax.axis_size("space")
    up = [(i, i + 1) for i in range(space_size - 1)]
    down = [(i + 1, i) for i in range(space_size - 1)]
    cond_own, drain_own = lookup_both(material, conductance, rock_heat_drain)
    tables_up = jnp.concatenate([cond_own[-halo:], drain_own[-halo:]], axis=0)
    tables_down = jnp.concatenate([cond_own[:halo], drain_own[:halo]], axis=0)
    tables_prev = lax.ppermute(tables_up, "space", up)
    tables_next = lax.ppermute(tables_down, "space", down)
    seeded_prev = lax.ppermute(seeded[-halo:], "space", up)
    seeded_next = lax.ppermute(seeded[:halo], "space", down)
    current = jnp.concatenate([seeded_prev, seeded, seeded_next], axis=0)
    cond_ext = jnp.concatenate([tables_prev[:halo], cond_own, tables_next[:halo]], axis=0)
    drain_ext = jnp.concatenate([tables_prev[halo:], drain_own, tables_next[halo:]], axis=0)
    extended = planes + 2 * halo
    plane = lax.axis_index("space") * planes - halo + lax.iota(jnp.int32, extended)
    inside = (plane >= 0) & (plane < space_size * planes)
    cond_ext = jnp.where(inside[:, None, None], cond_ext, 0.0)
    losses_ext = drain_ext + ventilation_heat_loss[0]
    for sweep_index in range(FINE_STEPS):
        lo, hi = sweep_index, extended - sweep_index
        weighted = cond_ext[lo:hi] * current
        x_sides = weighted[2:] + weighted[:-2]
        inner = weighted[1:-1]
        padded = jnp.pad(inner, ((0, 0), (1, 1), (1, 1)))
        y_sides = padded[:, 2:, 1:-1] + padded[:, :-2, 1:-1]
        z_sides = padded[:, 1:-1, 2:] + padded[:, 1:-1, :-2]
        kept = current[1:-1]
        current = kept + ((x_sides + y_sides + z_sides) - 6.0 * inner) - losses_ext[lo + 1 : hi - 1] * kept
    cell_heat_drain = drain_own
    coarse_baseline = coarsen(cell_heat_drain)
    coarse_decay_rate = jnp.exp(-FINE_STEPS * (coarse_baseline + ventilation_heat_loss[0]))
    coarse_old = coarsen(adjoint)
    correction = current - refine(coarse_decay_rate * coarse_old)
    reduced = coarsen(correction)
    tm_size = lax.axis_size("tm")
    is_last = lax.axis_index("tm") == tm_size - 1
    per_cell = jnp.exp(-FINE_STEPS * coarse_baseline)
    gain = jnp.exp(-FINE_STEPS * ventilation_heat_loss[0])
    top = coarse_decay_rate * coarse_old + reduced
    total = jnp.where(is_last, top, reduced)
    shape = total.shape
    width = shape[-1]
    rows = total.size // width
    packed = jnp.concatenate(
        [total.reshape(rows, width), jnp.broadcast_to(gain, (8, width))], axis=0
    )
    power = jnp.concatenate([per_cell.reshape(rows, width), jnp.ones((8, width), jnp.float32)], axis=0)
    is_field = lax.broadcasted_iota(jnp.int32, packed.shape, 0) < rows
    distance = 1
    while distance < tm_size:
        arrived = shifted(packed, "tm", -distance)
        own_gain = packed[rows, 0]
        packed = jnp.where(is_field, packed + (power * own_gain) * arrived, packed * arrived)
        power = power * power
        distance *= 2
    total = packed[:rows].reshape(shape)
    decayed = jnp.where(is_last, coarse_decay_rate * coarse_old, total - reduced)
    adjoint_new = refine(decayed) + correction
    return adjoint_new[None]


def solution(mesh):
    in_specs = (
        P("tm", "space", None, None),
        P("space", None, None),
        P("space"),
        P("tm", "space"),
        P("tm"),
        P(),
        P(),
    )
    out_specs = P("tm", "space", None, None)
    return jax.shard_map(
        on_device, mesh=mesh, in_specs=in_specs, out_specs=out_specs, check_vma=False
    )
```
